256 devices in a mesh: dp: 32 (over z, y), section: 4 (over x_lo, core), mp: 2 (over x_hi).
Axes of the slice: x: 4 (x_hi: 2, x_lo: 2; x = x_hi * 2 + x_lo), y: 4, z: 8, core: 2. Of those that a mesh axis runs over, the one named last changes fastest.
Arguments:
- arriving: bfloat16 [4, 4608, 8192], P('section', 'dp', 'mp'), may hold values from -6 to 6
- keep_mask: int32 [4608], P('dp'), may hold values 0 or 1
- mask_vector: bfloat16 [8192], P('mp'), may hold values from -5 to 5
- stashed: bfloat16 [4, 4608, 8192], P('section', 'dp', 'mp'), may hold values from -6 to 6
- cotangent: bfloat16 [4, 4608, 8192], P('section', 'dp', 'mp'), may hold values from -6 to 6
- gain: bfloat16 [4, 8192], P('section', 'mp'), may hold values from 0.3984375 to 1.59375
- down_adapter: bfloat16 [4, 8192, 256], P('section', None, 'mp'), may hold values from -0.0625 to 0.0625
- up_adapter: bfloat16 [4, 256, 8192], P('section', 'mp'), may hold values from -0.375 to 0.375
Outputs:
- next_input: bfloat16 [4, 4608, 8192], P('section', 'dp', 'mp')
- prev_grad: bfloat16 [4, 4608, 8192], P('section', 'dp', 'mp')
- down_grad: float32 [4, 8192, 256], P('section', 'dp', 'mp')
- up_grad: float32 [4, 256, 8192], P('section', 'mp', 'dp')
The draws below stay inside these ranges and needn't reach their ends.
All inputs are finite; a program needn't handle non-finite values. No bound on the sum of `keep_mask` on one device may be relied on, other than what follows from the above.
Results may differ from the reference program's by a relative error of at most 0.0015.
The reference program's roundings to bfloat16 on the way count: a program that leaves them out, or rounds other values in their place, can miss the bound.
Values may be sent and summed in bfloat16 or wider, within the bound.
No kernel may reach another device: no remote copies, remote signals or barrier semaphores. Data moves between devices by JAX's collectives and lax.ppermute only.
A program may use at most 128 MiB of HBM per device.

```python
import jax
import jax.numpy as jnp
from jax import lax

D = 8192
R = 256
TOKENS = 4608
SECTIONS = 4
N_DP = 32


def place_ends(entries, stream_key, smallest, top_value):
    shape = entries.shape
    index_at = [jax.random.randint(jax.random.fold_in(stream_key, axis), (), 0, shape[axis]) for axis in range(len(shape))]
    entries = entries.at[tuple(index_at)].set(smallest)
    longest = shape.index(max(shape))
    index_at[longest] = (index_at[longest] + 1) % shape[longest]
    return entries.at[tuple(index_at)].set(top_value)


def raised(drawn, own_key, source, target, blocks, factor):
    def block_of(axis_at):
        return (jnp.arange(drawn.shape[axis_at]) // (drawn.shape[axis_at] // blocks)).reshape((-1,) + (1,) * (drawn.ndim - 1 - axis_at))

    near = jax.random.permutation(own_key, blocks)[block_of(target)]
    far = (block_of(target) + blocks // 2) % blocks
    return jnp.where((block_of(source) == near) | (block_of(source) == far), factor * drawn, drawn)


def block_scale(own_key, dims, pieces, smallest, largest):
    def one(dim, blocks):
        draws = jax.random.uniform(jax.random.fold_in(jax.random.fold_in(own_key, 6), dim), (blocks,), jnp.float32, smallest / len(pieces), largest / len(pieces))
        return jnp.repeat(jnp.exp(draws), dims[dim] // blocks).reshape((-1,) + (1,) * (len(dims) - dim - 1))

    level = one(*pieces[0])
    for cut in pieces[1:]:
        level = level * one(*cut)
    return level


def noise(own_key, shape, deviation, limit, cuts=(), kind=jnp.bfloat16):
    level = block_scale(own_key, shape, cuts, -0.22, 0.18) if cuts else 1.0
    entries = jax.random.normal(own_key, shape, jnp.float32) * deviation * level
    return jnp.minimum(jnp.maximum(entries, -limit), limit).astype(kind)


def noise_with(own_key, shape, scale, limit, cuts, heavy, held_as=jnp.bfloat16):
    drawn = scale * jax.random.normal(own_key, shape, jnp.float32)
    if cuts:
        drawn = drawn * block_scale(own_key, shape, cuts, -0.22, 0.18)
    return jnp.clip(raised(drawn, jax.random.fold_in(own_key, 3), *heavy), -limit, limit).astype(held_as)


def setup_inputs(seed: int = 0) -> dict:
    splits = jax.random.split(jax.random.key(seed), 9)
    arriving = noise(splits[0], (SECTIONS, TOKENS, D), 1.0, 6.0, ((0, 4), (1, 32), (2, 2)))
    keep_mask = place_ends((jax.random.randint(splits[1], (TOKENS,), 0, 10) < 3).astype(jnp.int32), jax.random.fold_in(splits[1], 1), 0, 1)
    mask_vector = noise(splits[2], (D,), 1.0, 5.0, ((0, 2),))
    stashed = noise_with(splits[3], (SECTIONS, TOKENS, D), 1.0, 6.0, ((0, 4), (1, 32), (2, 2)), (1, 2, 32, 2.75))
    cotangent = noise_with(splits[4], (SECTIONS, TOKENS, D), 1.0, 6.0, ((0, 4), (1, 32), (2, 2)), (1, 2, 32, 2.75))
    gain = jnp.clip(1.0 + 0.12 * jax.random.normal(splits[5], (SECTIONS, D), jnp.float32), 0.3984375, 1.59375).astype(jnp.bfloat16)
    down_adapter = noise(splits[6], (SECTIONS, D, R), D ** -0.5, 0.0625, ((0, 4), (2, 2)))
    up_adapter = noise(splits[7], (SECTIONS, R, D), R ** -0.5, 0.375, ((0, 4), (1, 2)))
    return dict(arriving=arriving, keep_mask=keep_mask, mask_vector=mask_vector, stashed=stashed, cotangent=cotangent, gain=gain, down_adapter=down_adapter, up_adapter=up_adapter)


def row_scale(rows):
    values = rows.astype(jnp.float32)
    return lax.rsqrt(lax.optimization_barrier(jnp.mean(values * values, axis=1, keepdims=True)) + 1e-05)

def contract_rows(left, right):
    return lax.dot_general(left, right, (((0,), (0,)), ((), ())), preferred_element_type=jnp.float32)

def contract_cols(left, right):
    return lax.dot_general(left, right, (((1,), (1,)), ((), ())), preferred_element_type=jnp.float32)

def reference(arriving, keep_mask, mask_vector, stashed, cotangent, gain, down_adapter, up_adapter):
    outputs = []
    backs = []
    down_grads = []
    up_grads = []
    for position in range(SECTIONS):
        gain_row = gain[position].astype(jnp.float32)[None, :]
        inputs = arriving[position]
        if position == 0:
            inputs = jnp.where(keep_mask[:, None] == 1, inputs, mask_vector[None, :])
        normed = (inputs.astype(jnp.float32) * row_scale(inputs) * gain_row).astype(jnp.bfloat16)
        hidden_pre = jnp.dot(normed, down_adapter[position], preferred_element_type=jnp.float32)
        hidden = jax.nn.silu(hidden_pre).astype(jnp.bfloat16)
        branch = jnp.dot(hidden, up_adapter[position], preferred_element_type=jnp.float32)
        outputs.append((inputs.astype(jnp.float32) + branch).astype(jnp.bfloat16))
        saved = stashed[position]
        upstream = cotangent[position]
        saved_scale = row_scale(saved)
        saved_values = saved.astype(jnp.float32)
        saved_normed = (saved_values * saved_scale * gain_row).astype(jnp.bfloat16)
        saved_pre = jnp.dot(saved_normed, down_adapter[position], preferred_element_type=jnp.float32)
        sigmoid_pre = jax.nn.sigmoid(saved_pre)
        saved_hidden = (saved_pre * sigmoid_pre).astype(jnp.bfloat16)
        hidden_grad = contract_cols(upstream, up_adapter[position])
        pre_grad = (hidden_grad * sigmoid_pre * (1.0 + saved_pre * (1.0 - sigmoid_pre))).astype(jnp.bfloat16)
        normed_grad = contract_cols(pre_grad, down_adapter[position])
        scaled_grad = normed_grad * gain_row
        row_dot = lax.optimization_barrier(jnp.sum(saved_values * scaled_grad, axis=1, keepdims=True))
        cubed = saved_scale * saved_scale * saved_scale
        input_grad = upstream.astype(jnp.float32) + saved_scale * scaled_grad - saved_values * cubed * (row_dot / D)
        backs.append(input_grad.astype(jnp.bfloat16))
        down_grads.append(contract_rows(saved_normed, pre_grad) / N_DP)
        up_grads.append(contract_rows(saved_hidden, upstream) / N_DP)
    zeros = jnp.zeros_like(arriving[0])
    next_input = jnp.stack([zeros] + outputs[:-1])
    prev_grad = jnp.stack(backs[1:] + [zeros])
    return (next_input, prev_grad, jnp.stack(down_grads), jnp.stack(up_grads))
```

```python
import jax
import jax.numpy as jnp
from jax import lax
from jax.sharding import PartitionSpec as P


def shifted(shard, axis, by):
    peers = lax.axis_size(axis)
    pairs = [(i, i + by) for i in range(peers) if 0 <= i + by < peers]
    return lax.ppermute(shard, axis, pairs)


def swapped(shard, axis):
    return lax.ppermute(shard, axis, [(0, 1), (1, 0)])


def contract_rows(left, right):
    return lax.dot_general(
        left, right, (((0,), (0,)), ((), ())), preferred_element_type=jnp.float32
    )


def contract_cols(left, right):
    return lax.dot_general(
        left, right, (((1,), (1,)), ((), ())), preferred_element_type=jnp.float32
    )


def in_unit_order(own, received, first, axis):
    return jnp.where(
        first,
        jnp.concatenate([own, received], axis=axis),
        jnp.concatenate([received, own], axis=axis),
    )


def on_device(arriving, keep_mask, mask_vector, stashed, cotangent, gain, down_adapter, up_adapter):
    half = lax.axis_index("mp")
    first = half == 0
    is_first = lax.axis_index("section") == 0
    kept_rows = jnp.logical_or(keep_mask == 1, jnp.logical_not(is_first))
    inputs = jnp.where(kept_rows[:, None], arriving[0], mask_vector[None, :])
    saved = stashed[0]
    upstream = cotangent[0]
    gain_row = gain[0].astype(jnp.float32)[None, :]
    down_local = down_adapter[0]
    up_local = up_adapter[0]
    width = inputs.shape[1]
    full_width = width * lax.axis_size("mp")
    replicas = lax.axis_size("dp")

    down_mine = lax.dynamic_slice_in_dim(down_local, half * width, width, axis=0)
    down_theirs = lax.dynamic_slice_in_dim(down_local, (1 - half) * width, width, axis=0)
    up_mine = lax.dynamic_slice_in_dim(up_local, half * width, width, axis=1)
    up_theirs = lax.dynamic_slice_in_dim(up_local, (1 - half) * width, width, axis=1)
    down_half = in_unit_order(down_mine, swapped(down_theirs, "mp"), first, 1)
    up_half = in_unit_order(up_mine, swapped(up_theirs, "mp"), first, 0)

    input_values = inputs.astype(jnp.float32)
    saved_values = saved.astype(jnp.float32)
    squares = lax.psum(
        jnp.stack(
            [jnp.sum(input_values * input_values, axis=1), jnp.sum(saved_values * saved_values, axis=1)]
        ),
        "mp",
    )
    scale = lax.rsqrt(squares[0] / full_width + 1e-05)[:, None]
    saved_scale = lax.rsqrt(squares[1] / full_width + 1e-05)[:, None]
    normed = (input_values * scale * gain_row).astype(jnp.bfloat16)
    saved_normed = (saved_values * saved_scale * gain_row).astype(jnp.bfloat16)

    partials = lax.psum(
        jnp.stack(
            [
                jnp.dot(normed, down_half, preferred_element_type=jnp.float32),
                jnp.dot(saved_normed, down_half, preferred_element_type=jnp.float32),
                contract_cols(upstream, up_half),
            ]
        ),
        "mp",
    )
    hidden_pre, saved_pre, hidden_grad = partials[0], partials[1], partials[2]
    hidden = jax.nn.silu(hidden_pre).astype(jnp.bfloat16)
    branch = jnp.dot(hidden, up_half, preferred_element_type=jnp.float32)
    output = (input_values + branch).astype(jnp.bfloat16)

    sigmoid_pre = jax.nn.sigmoid(saved_pre)
    saved_hidden = (saved_pre * sigmoid_pre).astype(jnp.bfloat16)
    pre_grad = (hidden_grad * sigmoid_pre * (1.0 + saved_pre * (1.0 - sigmoid_pre))).astype(
        jnp.bfloat16
    )
    scaled_grad = contract_cols(pre_grad, down_half) * gain_row
    row_dot = lax.psum(jnp.sum(saved_values * scaled_grad, axis=1), "mp")
    cubed = saved_scale * saved_scale * saved_scale
    input_grad = (
        upstream.astype(jnp.float32)
        + saved_scale * scaled_grad
        - saved_values * cubed * (row_dot[:, None] / full_width)
    ).astype(jnp.bfloat16)
    next_input = shifted(output, "section", 1)
    prev_grad = shifted(input_grad, "section", -1)

    blocks = replicas // 2
    units = down_local.shape[1]
    down_part = contract_rows(saved_normed, pre_grad)
    up_part = contract_rows(saved_hidden, upstream)
    down_slots = (
        down_part.reshape(blocks, full_width // replicas, 2, units)
        .transpose(2, 0, 1, 3)
        .reshape(replicas, -1)
    )
    up_slots = (
        up_part.reshape(2, units, blocks, full_width // replicas)
        .transpose(0, 2, 1, 3)
        .reshape(replicas, -1)
    )
    lanes = 128
    slots = jnp.concatenate([down_slots, up_slots], axis=1).reshape(replicas, -1, lanes)
    summed = lax.all_to_all(slots, "dp", 0, 0, tiled=True).sum(axis=0).reshape(-1)
    slot = lax.axis_index("dp")
    keeps = (slot // blocks) == half
    pairs = []
    for j in range(replicas):
        for m in range(2):
            if j // blocks != m:
                pairs.append((j * 2 + m, (j ^ blocks) * 2 + (1 - m)))
    moved = lax.ppermute(summed, ("dp", "mp"), pairs)
    mine = jnp.where(keeps, summed, moved) * (1.0 / replicas)
    down_grad = mine[: down_slots.shape[1]].reshape(full_width // replicas, units)
    up_grad = mine[down_slots.shape[1] :].reshape(units, full_width // replicas)
    return (next_input[None], prev_grad[None], down_grad[None], up_grad[None])


def solution(mesh):
    placed = (
        P("section", "dp", "mp"),
        P("dp"),
        P("mp"),
        P("section", "dp", "mp"),
        P("section", "dp", "mp"),
        P("section", "mp"),
        P("section", None, "mp"),
        P("section", "mp", None),
    )
    return jax.shard_map(
        on_device,
        mesh=mesh,
        in_specs=placed,
        out_specs=(
            P("section", "dp", "mp"),
            P("section", "dp", "mp"),
            P("section", "dp", "mp"),
            P("section", "mp", "dp"),
        ),
        check_vma=False,
    )
```

```python
import jax
import jax.numpy as jnp
from jax import lax
from jax.sharding import PartitionSpec as P


def shifted(shard, axis, by):
    peers = lax.axis_size(axis)
    pairs = [(i, i + by) for i in range(peers) if 0 <= i + by < peers]
    return lax.ppermute(shard, axis, pairs)


def swapped(shard, axis):
    return lax.ppermute(shard, axis, [(0, 1), (1, 0)])


def pair_sum(shard, axis):
    return shard + swapped(shard, axis)


def contract_rows(left, right):
    return lax.dot_general(
        left, right, (((0,), (0,)), ((), ())), preferred_element_type=jnp.float32
    )


def contract_cols(left, right):
    return lax.dot_general(
        left, right, (((1,), (1,)), ((), ())), preferred_element_type=jnp.float32
    )


def in_unit_order(own, received, first, axis):
    return jnp.where(
        first,
        jnp.concatenate([own, received], axis=axis),
        jnp.concatenate([received, own], axis=axis),
    )


def on_device(arriving, keep_mask, mask_vector, stashed, cotangent, gain, down_adapter, up_adapter):
    half = lax.axis_index("mp")
    first = half == 0
    is_first = lax.axis_index("section") == 0
    kept_rows = jnp.logical_or(keep_mask == 1, jnp.logical_not(is_first))
    inputs = jnp.where(kept_rows[:, None], arriving[0], mask_vector[None, :])
    saved = stashed[0]
    upstream = cotangent[0]
    gain_row = gain[0].astype(jnp.float32)[None, :]
    down_local = down_adapter[0]
    up_local = up_adapter[0]
    width = inputs.shape[1]
    full_width = width * lax.axis_size("mp")
    replicas = lax.axis_size("dp")

    down_mine = lax.dynamic_slice_in_dim(down_local, half * width, width, axis=0)
    down_theirs = lax.dynamic_slice_in_dim(down_local, (1 - half) * width, width, axis=0)
    up_mine = lax.dynamic_slice_in_dim(up_local, half * width, width, axis=1)
    up_theirs = lax.dynamic_slice_in_dim(up_local, (1 - half) * width, width, axis=1)
    down_half = in_unit_order(down_mine, swapped(down_theirs, "mp"), first, 1)
    up_half = in_unit_order(up_mine, swapped(up_theirs, "mp"), first, 0)

    input_values = inputs.astype(jnp.float32)
    saved_values = saved.astype(jnp.float32)
    squares = pair_sum(
        jnp.stack(
            [jnp.sum(input_values * input_values, axis=1), jnp.sum(saved_values * saved_values, axis=1)]
        ),
        "mp",
    )
    scale = lax.rsqrt(squares[0] / full_width + 1e-05)[:, None]
    saved_scale = lax.rsqrt(squares[1] / full_width + 1e-05)[:, None]
    normed = (input_values * scale * gain_row).astype(jnp.bfloat16)
    saved_normed = (saved_values * saved_scale * gain_row).astype(jnp.bfloat16)

    partials = pair_sum(
        jnp.stack(
            [
                jnp.dot(normed, down_half, preferred_element_type=jnp.float32),
                jnp.dot(saved_normed, down_half, preferred_element_type=jnp.float32),
                contract_cols(upstream, up_half),
            ]
        ),
        "mp",
    )
    hidden_pre, saved_pre, hidden_grad = partials[0], partials[1], partials[2]
    hidden = jax.nn.silu(hidden_pre).astype(jnp.bfloat16)
    branch = jnp.dot(hidden, up_half, preferred_element_type=jnp.float32)
    output = (input_values + branch).astype(jnp.bfloat16)

    sigmoid_pre = jax.nn.sigmoid(saved_pre)
    saved_hidden = (saved_pre * sigmoid_pre).astype(jnp.bfloat16)
    pre_grad = (hidden_grad * sigmoid_pre * (1.0 + saved_pre * (1.0 - sigmoid_pre))).astype(
        jnp.bfloat16
    )
    scaled_grad = contract_cols(pre_grad, down_half) * gain_row
    row_dot = pair_sum(jnp.sum(saved_values * scaled_grad, axis=1), "mp")
    cubed = saved_scale * saved_scale * saved_scale
    input_grad = (
        upstream.astype(jnp.float32)
        + saved_scale * scaled_grad
        - saved_values * cubed * (row_dot[:, None] / full_width)
    ).astype(jnp.bfloat16)
    next_input = shifted(output, "section", 1)
    prev_grad = shifted(input_grad, "section", -1)

    blocks = replicas // 2
    units = down_local.shape[1]
    down_part = contract_rows(saved_normed, pre_grad)
    up_part = contract_rows(saved_hidden, upstream)
    down_slots = (
        down_part.reshape(blocks, full_width // replicas, 2, units)
        .transpose(2, 0, 1, 3)
        .reshape(replicas, -1)
    )
    up_slots = (
        up_part.reshape(2, units, blocks, full_width // replicas)
        .transpose(0, 2, 1, 3)
        .reshape(replicas, -1)
    )
    lanes = 128
    slots = jnp.concatenate([down_slots, up_slots], axis=1).reshape(replicas, -1, lanes)
    summed = lax.all_to_all(slots, "dp", 0, 0, tiled=True).sum(axis=0).reshape(-1)
    slot = lax.axis_index("dp")
    keeps = (slot // blocks) == half
    pairs = []
    for j in range(replicas):
        for m in range(2):
            if j // blocks != m:
                pairs.append((j * 2 + m, (j ^ blocks) * 2 + (1 - m)))
    moved = lax.ppermute(summed, ("dp", "mp"), pairs)
    mine = jnp.where(keeps, summed, moved) * (1.0 / replicas)
    down_grad = mine[: down_slots.shape[1]].reshape(full_width // replicas, units)
    up_grad = mine[down_slots.shape[1] :].reshape(units, full_width // replicas)
    return (next_input[None], prev_grad[None], down_grad[None], up_grad[None])


def solution(mesh):
    placed = (
        P("section", "dp", "mp"),
        P("dp"),
        P("mp"),
        P("section", "dp", "mp"),
        P("section", "dp", "mp"),
        P("section", "mp"),
        P("section", None, "mp"),
        P("section", "mp", None),
    )
    return jax.shard_map(
        on_device,
        mesh=mesh,
        in_specs=placed,
        out_specs=(
            P("section", "dp", "mp"),
            P("section", "dp", "mp"),
            P("section", "dp", "mp"),
            P("section", "mp", "dp"),
        ),
        check_vma=False,
    )
```

```python
import jax
import jax.numpy as jnp
from jax import lax
from jax.sharding import PartitionSpec as P


def shifted(shard, axis, by):
    peers = lax.axis_size(axis)
    pairs = [(i, i + by) for i in range(peers) if 0 <= i + by < peers]
    return lax.ppermute(shard, axis, pairs)


def swapped(shard, axis):
    return lax.ppermute(shard, axis, [(0, 1), (1, 0)])


def pair_sum(shard, axis):
    return shard + swapped(shard, axis)


def contract_rows(left, right):
    return lax.dot_general(
        left, right, (((0,), (0,)), ((), ())), preferred_element_type=jnp.float32
    )


def contract_cols(left, right):
    return lax.dot_general(
        left, right, (((1,), (1,)), ((), ())), preferred_element_type=jnp.float32
    )


def in_unit_order(own, received, first, axis):
    return jnp.where(
        first,
        jnp.concatenate([own, received], axis=axis),
        jnp.concatenate([received, own], axis=axis),
    )


def on_device(arriving, keep_mask, mask_vector, stashed, cotangent, gain, down_adapter, up_adapter):
    half = lax.axis_index("mp")
    first = half == 0
    is_first = lax.axis_index("section") == 0
    kept_rows = jnp.logical_or(keep_mask == 1, jnp.logical_not(is_first))
    inputs = jnp.where(kept_rows[:, None], arriving[0], mask_vector[None, :])
    saved = stashed[0]
    upstream = cotangent[0]
    gain_row = gain[0].astype(jnp.float32)[None, :]
    down_local = down_adapter[0]
    up_local = up_adapter[0]
    width = inputs.shape[1]
    full_width = width * lax.axis_size("mp")
    replicas = lax.axis_size("dp")

    down_mine = lax.dynamic_slice_in_dim(down_local, half * width, width, axis=0)
    down_theirs = lax.dynamic_slice_in_dim(down_local, (1 - half) * width, width, axis=0)
    up_mine = lax.dynamic_slice_in_dim(up_local, half * width, width, axis=1)
    up_theirs = lax.dynamic_slice_in_dim(up_local, (1 - half) * width, width, axis=1)
    down_half = in_unit_order(down_mine, swapped(down_theirs, "mp"), first, 1)
    up_half = in_unit_order(up_mine, swapped(up_theirs, "mp"), first, 0)

    input_values = inputs.astype(jnp.float32)
    saved_values = saved.astype(jnp.float32)
    squares = pair_sum(
        jnp.stack(
            [jnp.sum(input_values * input_values, axis=1), jnp.sum(saved_values * saved_values, axis=1)]
        ),
        "mp",
    )
    scale = lax.rsqrt(squares[0] / full_width + 1e-05)[:, None]
    saved_scale = lax.rsqrt(squares[1] / full_width + 1e-05)[:, None]
    normed = (input_values * scale * gain_row).astype(jnp.bfloat16)
    saved_normed = (saved_values * saved_scale * gain_row).astype(jnp.bfloat16)

    partials = pair_sum(
        jnp.stack(
            [
                jnp.dot(normed, down_half, preferred_element_type=jnp.float32),
                jnp.dot(saved_normed, down_half, preferred_element_type=jnp.float32),
                contract_cols(upstream, up_half),
            ]
        ),
        "mp",
    )
    hidden_pre, saved_pre, hidden_grad = partials[0], partials[1], partials[2]
    hidden = jax.nn.silu(hidden_pre).astype(jnp.bfloat16)
    branch = jnp.dot(hidden, up_half, preferred_element_type=jnp.float32)
    output = (input_values + branch).astype(jnp.bfloat16)

    sigmoid_pre = jax.nn.sigmoid(saved_pre)
    saved_hidden = (saved_pre * sigmoid_pre).astype(jnp.bfloat16)
    pre_grad = (hidden_grad * sigmoid_pre * (1.0 + saved_pre * (1.0 - sigmoid_pre))).astype(
        jnp.bfloat16
    )
    scaled_grad = contract_cols(pre_grad, down_half) * gain_row
    row_dot = pair_sum(jnp.sum(saved_values * scaled_grad, axis=1), "mp")
    cubed = saved_scale * saved_scale * saved_scale
    input_grad = (
        upstream.astype(jnp.float32)
        + saved_scale * scaled_grad
        - saved_values * cubed * (row_dot[:, None] / full_width)
    ).astype(jnp.bfloat16)
    next_input = shifted(output, "section", 1)
    prev_grad = shifted(input_grad, "section", -1)

    blocks = replicas // 2
    units = down_local.shape[1]
    block = full_width // replicas
    ny = 4
    nz = replicas // ny
    down_part = contract_rows(saved_normed, pre_grad)
    up_part = contract_rows(saved_hidden, upstream)
    down_slots = (
        down_part.reshape(nz // 2, ny, block, 2, units)
        .transpose(1, 3, 0, 2, 4)
        .reshape(ny, nz, block * units)
    )
    up_slots = (
        up_part.reshape(2, units, nz // 2, ny, block)
        .transpose(3, 0, 2, 1, 4)
        .reshape(ny, nz, units * block)
    )
    lanes = 128
    slots = jnp.concatenate([down_slots, up_slots], axis=2)
    y_groups = [[z * ny + y for y in range(ny)] for z in range(nz)]
    z_groups = [[z * ny + y for z in range(nz)] for y in range(ny)]
    over_y = lax.all_to_all(
        slots.reshape(ny, -1, lanes), "dp", 0, 0, tiled=True, axis_index_groups=y_groups
    ).sum(axis=0)
    summed = (
        lax.all_to_all(
            over_y.reshape(nz, -1, lanes), "dp", 0, 0, tiled=True, axis_index_groups=z_groups
        )
        .sum(axis=0)
        .reshape(-1)
    )
    slot = lax.axis_index("dp")
    keeps = (slot // blocks) == half
    pairs = []
    for j in range(replicas):
        for m in range(2):
            if j // blocks != m:
                pairs.append((j * 2 + m, (j ^ blocks) * 2 + (1 - m)))
    moved = lax.ppermute(summed, ("dp", "mp"), pairs)
    mine = jnp.where(keeps, summed, moved) * (1.0 / replicas)
    down_grad = mine[: block * units].reshape(block, units)
    up_grad = mine[block * units :].reshape(units, block)
    return (next_input[None], prev_grad[None], down_grad[None], up_grad[None])


def solution(mesh):
    placed = (
        P("section", "dp", "mp"),
        P("dp"),
        P("mp"),
        P("section", "dp", "mp"),
        P("section", "dp", "mp"),
        P("section", "mp"),
        P("section", None, "mp"),
        P("section", "mp", None),
    )
    return jax.shard_map(
        on_device,
        mesh=mesh,
        in_specs=placed,
        out_specs=(
            P("section", "dp", "mp"),
            P("section", "dp", "mp"),
            P("section", "dp", "mp"),
            P("section", "mp", "dp"),
        ),
        check_vma=False,
    )
```

```python
import jax
import jax.numpy as jnp
from jax import lax
from jax.sharding import PartitionSpec as P


def shifted(shard, axis, by):
    peers = lax.axis_size(axis)
    pairs = [(i, i + by) for i in range(peers) if 0 <= i + by < peers]
    return lax.ppermute(shard, axis, pairs)


def swapped(shard, axis):
    return lax.ppermute(shard, axis, [(0, 1), (1, 0)])


def pair_sum(shard, axis):
    return shard + swapped(shard, axis)


def contract_rows(left, right):
    return lax.dot_general(
        left, right, (((0,), (0,)), ((), ())), preferred_element_type=jnp.float32
    )


def contract_cols(left, right):
    return lax.dot_general(
        left, right, (((1,), (1,)), ((), ())), preferred_element_type=jnp.float32
    )


def in_unit_order(own, received, first, axis):
    return jnp.where(
        first,
        jnp.concatenate([own, received], axis=axis),
        jnp.concatenate([received, own], axis=axis),
    )


def on_device(arriving, keep_mask, mask_vector, stashed, cotangent, gain, down_adapter, up_adapter):
    half = lax.axis_index("mp")
    first = half == 0
    is_first = lax.axis_index("section") == 0
    kept_rows = jnp.logical_or(keep_mask == 1, jnp.logical_not(is_first))
    inputs = jnp.where(kept_rows[:, None], arriving[0], mask_vector[None, :])
    saved = stashed[0]
    upstream = cotangent[0]
    gain_row = gain[0].astype(jnp.float32)[None, :]
    down_local = down_adapter[0]
    up_local = up_adapter[0]
    width = inputs.shape[1]
    full_width = width * lax.axis_size("mp")
    replicas = lax.axis_size("dp")

    down_mine = lax.dynamic_slice_in_dim(down_local, half * width, width, axis=0)
    down_theirs = lax.dynamic_slice_in_dim(down_local, (1 - half) * width, width, axis=0)
    up_mine = lax.dynamic_slice_in_dim(up_local, half * width, width, axis=1)
    up_theirs = lax.dynamic_slice_in_dim(up_local, (1 - half) * width, width, axis=1)
    down_half = in_unit_order(down_mine, swapped(down_theirs, "mp"), first, 1)
    up_half = in_unit_order(up_mine, swapped(up_theirs, "mp"), first, 0)

    input_values = inputs.astype(jnp.float32)
    saved_values = saved.astype(jnp.float32)
    squares = pair_sum(
        jnp.stack(
            [jnp.sum(input_values * input_values, axis=1), jnp.sum(saved_values * saved_values, axis=1)]
        ),
        "mp",
    )
    scale = lax.rsqrt(squares[0] / full_width + 1e-05)[:, None]
    saved_scale = lax.rsqrt(squares[1] / full_width + 1e-05)[:, None]
    normed = (input_values * scale * gain_row).astype(jnp.bfloat16)
    saved_normed = (saved_values * saved_scale * gain_row).astype(jnp.bfloat16)

    partials = pair_sum(
        jnp.stack(
            [
                jnp.dot(normed, down_half, preferred_element_type=jnp.float32),
                jnp.dot(saved_normed, down_half, preferred_element_type=jnp.float32),
                contract_cols(upstream, up_half),
            ]
        ),
        "mp",
    )
    hidden_pre, saved_pre, hidden_grad = partials[0], partials[1], partials[2]
    hidden = jax.nn.silu(hidden_pre).astype(jnp.bfloat16)
    branch = jnp.dot(hidden, up_half, preferred_element_type=jnp.float32)
    output = (input_values + branch).astype(jnp.bfloat16)

    sigmoid_pre = jax.nn.sigmoid(saved_pre)
    saved_hidden = (saved_pre * sigmoid_pre).astype(jnp.bfloat16)
    pre_grad = (hidden_grad * sigmoid_pre * (1.0 + saved_pre * (1.0 - sigmoid_pre))).astype(
        jnp.bfloat16
    )
    scaled_grad = contract_cols(pre_grad, down_half) * gain_row
    row_dot = pair_sum(jnp.sum(saved_values * scaled_grad, axis=1), "mp")
    cubed = saved_scale * saved_scale * saved_scale
    input_grad = (
        upstream.astype(jnp.float32)
        + saved_scale * scaled_grad
        - saved_values * cubed * (row_dot[:, None] / full_width)
    ).astype(jnp.bfloat16)
    next_input = shifted(output, "section", 1)
    prev_grad = shifted(input_grad, "section", -1)

    blocks = replicas // 2
    units = down_local.shape[1]
    block = full_width // replicas
    ny = 4
    nz = replicas // ny
    tokens = saved.shape[0]
    rows = jnp.stack([saved_normed, upstream])
    rows = rows.reshape(2, tokens, nz // 2, ny, block).transpose(3, 2, 0, 1, 4)
    rows = jnp.broadcast_to(rows[:, None], (ny, 2, nz // 2, 2, tokens, block))
    cols = jnp.stack([pre_grad, saved_hidden])
    cols = cols.reshape(2, tokens, 2, units).transpose(2, 0, 1, 3)
    cols = jnp.broadcast_to(cols[None, :, None], (ny, 2, nz // 2, 2, tokens, units))
    slots = lax.dot_general(
        rows, cols, (((4,), (4,)), ((0, 1, 2, 3), (0, 1, 2, 3))), preferred_element_type=jnp.float32
    )
    y_groups = [[z * ny + y for y in range(ny)] for z in range(nz)]
    z_groups = [[z * ny + y for z in range(nz)] for y in range(ny)]
    over_y = lax.all_to_all(
        slots, "dp", 0, 0, tiled=True, axis_index_groups=y_groups
    ).sum(axis=0)
    summed = lax.all_to_all(
        over_y.reshape(nz, 2, block, units), "dp", 0, 0, tiled=True, axis_index_groups=z_groups
    ).sum(axis=0)
    slot = lax.axis_index("dp")
    keeps = (slot // blocks) == half
    pairs = []
    for j in range(replicas):
        for m in range(2):
            if j // blocks != m:
                pairs.append((j * 2 + m, (j ^ blocks) * 2 + (1 - m)))
    moved = lax.ppermute(summed, ("dp", "mp"), pairs)
    mine = jnp.where(keeps, summed, moved) * (1.0 / replicas)
    down_grad = mine[0]
    up_grad = mine[1].T
    return (next_input[None], prev_grad[None], down_grad[None], up_grad[None])


def solution(mesh):
    placed = (
        P("section", "dp", "mp"),
        P("dp"),
        P("mp"),
        P("section", "dp", "mp"),
        P("section", "dp", "mp"),
        P("section", "mp"),
        P("section", None, "mp"),
        P("section", "mp", None),
    )
    return jax.shard_map(
        on_device,
        mesh=mesh,
        in_specs=placed,
        out_specs=(
            P("section", "dp", "mp"),
            P("section", "dp", "mp"),
            P("section", "dp", "mp"),
            P("section", "mp", "dp"),
        ),
        check_vma=False,
    )
```

```python
import jax
import jax.numpy as jnp
from jax import lax
from jax.sharding import PartitionSpec as P


def shifted(shard, axis, by):
    peers = lax.axis_size(axis)
    pairs = [(i, i + by) for i in range(peers) if 0 <= i + by < peers]
    return lax.ppermute(shard, axis, pairs)


def swapped(shard, axis):
    return lax.ppermute(shard, axis, [(0, 1), (1, 0)])


def pair_sum(shard, axis):
    return shard + swapped(shard, axis)


def contract_rows(left, right):
    return lax.dot_general(
        left, right, (((0,), (0,)), ((), ())), preferred_element_type=jnp.float32
    )


def contract_cols(left, right):
    return lax.dot_general(
        left, right, (((1,), (1,)), ((), ())), preferred_element_type=jnp.float32
    )


def around_x(sections, step):
    pairs = []
    for section in range(sections):
        for half in range(2):
            x = half * 2 + section // 2
            to = (x + step) % 4
            pairs.append((section * 2 + half, ((to % 2) * 2 + section % 2) * 2 + to // 2))
    return pairs


def in_unit_order(own, received, first, axis):
    return jnp.where(
        first,
        jnp.concatenate([own, received], axis=axis),
        jnp.concatenate([received, own], axis=axis),
    )


def on_device(arriving, keep_mask, mask_vector, stashed, cotangent, gain, down_adapter, up_adapter):
    half = lax.axis_index("mp")
    first = half == 0
    is_first = lax.axis_index("section") == 0
    kept_rows = jnp.logical_or(keep_mask == 1, jnp.logical_not(is_first))
    inputs = jnp.where(kept_rows[:, None], arriving[0], mask_vector[None, :])
    saved = stashed[0]
    upstream = cotangent[0]
    gain_row = gain[0].astype(jnp.float32)[None, :]
    down_local = down_adapter[0]
    up_local = up_adapter[0]
    width = inputs.shape[1]
    full_width = width * lax.axis_size("mp")
    replicas = lax.axis_size("dp")

    down_mine = lax.dynamic_slice_in_dim(down_local, half * width, width, axis=0)
    down_theirs = lax.dynamic_slice_in_dim(down_local, (1 - half) * width, width, axis=0)
    up_mine = lax.dynamic_slice_in_dim(up_local, half * width, width, axis=1)
    up_theirs = lax.dynamic_slice_in_dim(up_local, (1 - half) * width, width, axis=1)
    relay = around_x(lax.axis_size("section"), -1)
    up_received = lax.ppermute(
        lax.ppermute(up_theirs, ("section", "mp"), relay), ("section", "mp"), relay
    )
    down_half = in_unit_order(down_mine, swapped(down_theirs, "mp"), first, 1)
    up_half = in_unit_order(up_mine, up_received, first, 0)

    input_values = inputs.astype(jnp.float32)
    saved_values = saved.astype(jnp.float32)
    squares = pair_sum(
        jnp.stack(
            [jnp.sum(input_values * input_values, axis=1), jnp.sum(saved_values * saved_values, axis=1)]
        ),
        "mp",
    )
    scale = lax.rsqrt(squares[0] / full_width + 1e-05)[:, None]
    saved_scale = lax.rsqrt(squares[1] / full_width + 1e-05)[:, None]
    normed = (input_values * scale * gain_row).astype(jnp.bfloat16)
    saved_normed = (saved_values * saved_scale * gain_row).astype(jnp.bfloat16)

    partials = pair_sum(
        jnp.stack(
            [
                jnp.dot(normed, down_half, preferred_element_type=jnp.float32),
                jnp.dot(saved_normed, down_half, preferred_element_type=jnp.float32),
                contract_cols(upstream, up_half),
            ]
        ),
        "mp",
    )
    hidden_pre, saved_pre, hidden_grad = partials[0], partials[1], partials[2]
    hidden = jax.nn.silu(hidden_pre).astype(jnp.bfloat16)
    branch = jnp.dot(hidden, up_half, preferred_element_type=jnp.float32)
    output = (input_values + branch).astype(jnp.bfloat16)

    sigmoid_pre = jax.nn.sigmoid(saved_pre)
    saved_hidden = (saved_pre * sigmoid_pre).astype(jnp.bfloat16)
    pre_grad = (hidden_grad * sigmoid_pre * (1.0 + saved_pre * (1.0 - sigmoid_pre))).astype(
        jnp.bfloat16
    )
    scaled_grad = contract_cols(pre_grad, down_half) * gain_row
    row_dot = pair_sum(jnp.sum(saved_values * scaled_grad, axis=1), "mp")
    cubed = saved_scale * saved_scale * saved_scale
    input_grad = (
        upstream.astype(jnp.float32)
        + saved_scale * scaled_grad
        - saved_values * cubed * (row_dot[:, None] / full_width)
    ).astype(jnp.bfloat16)
    next_input = shifted(output, "section", 1)
    prev_grad = shifted(input_grad, "section", -1)

    blocks = replicas // 2
    units = down_local.shape[1]
    block = full_width // replicas
    ny = 4
    nz = replicas // ny
    tokens = saved.shape[0]
    rows = jnp.stack([saved_normed, upstream])
    rows = rows.reshape(2, tokens, nz // 2, ny, block).transpose(3, 2, 0, 1, 4)
    rows = jnp.broadcast_to(rows[:, None], (ny, 2, nz // 2, 2, tokens, block))
    cols = jnp.stack([pre_grad, saved_hidden])
    cols = cols.reshape(2, tokens, 2, units).transpose(2, 0, 1, 3)
    cols = jnp.broadcast_to(cols[None, :, None], (ny, 2, nz // 2, 2, tokens, units))
    slots = lax.dot_general(
        rows, cols, (((4,), (4,)), ((0, 1, 2, 3), (0, 1, 2, 3))), preferred_element_type=jnp.float32
    )
    y_groups = [[z * ny + y for y in range(ny)] for z in range(nz)]
    z_groups = [[z * ny + y for z in range(nz)] for y in range(ny)]
    over_y = lax.all_to_all(
        slots, "dp", 0, 0, tiled=True, axis_index_groups=y_groups
    ).sum(axis=0)
    summed = lax.all_to_all(
        over_y.reshape(nz, 2, block, units), "dp", 0, 0, tiled=True, axis_index_groups=z_groups
    ).sum(axis=0)
    slot = lax.axis_index("dp")
    keeps = (slot // blocks) == half
    pairs = []
    for j in range(replicas):
        for m in range(2):
            if j // blocks != m:
                pairs.append((j * 2 + m, (j ^ blocks) * 2 + (1 - m)))
    moved = lax.ppermute(summed, ("dp", "mp"), pairs)
    mine = jnp.where(keeps, summed, moved) * (1.0 / replicas)
    down_grad = mine[0]
    up_grad = mine[1].T
    return (next_input[None], prev_grad[None], down_grad[None], up_grad[None])


def solution(mesh):
    placed = (
        P("section", "dp", "mp"),
        P("dp"),
        P("mp"),
        P("section", "dp", "mp"),
        P("section", "dp", "mp"),
        P("section", "mp"),
        P("section", None, "mp"),
        P("section", "mp", None),
    )
    return jax.shard_map(
        on_device,
        mesh=mesh,
        in_specs=placed,
        out_specs=(
            P("section", "dp", "mp"),
            P("section", "dp", "mp"),
            P("section", "dp", "mp"),
            P("section", "mp", "dp"),
        ),
        check_vma=False,
    )
```

```python
import jax
import jax.numpy as jnp
from jax import lax
from jax.sharding import PartitionSpec as P


def shifted(shard, axis, by):
    peers = lax.axis_size(axis)
    pairs = [(i, i + by) for i in range(peers) if 0 <= i + by < peers]
    return lax.ppermute(shard, axis, pairs)


def swapped(shard, axis):
    return lax.ppermute(shard, axis, [(0, 1), (1, 0)])


def pair_sum(shard, axis):
    return shard + swapped(shard, axis)


def contract_rows(left, right):
    return lax.dot_general(
        left, right, (((0,), (0,)), ((), ())), preferred_element_type=jnp.float32
    )


def contract_cols(left, right):
    return lax.dot_general(
        left, right, (((1,), (1,)), ((), ())), preferred_element_type=jnp.float32
    )


def in_unit_order(own, received, first, axis):
    return jnp.where(
        first,
        jnp.concatenate([own, received], axis=axis),
        jnp.concatenate([received, own], axis=axis),
    )


def on_device(arriving, keep_mask, mask_vector, stashed, cotangent, gain, down_adapter, up_adapter):
    half = lax.axis_index("mp")
    first = half == 0
    is_first = lax.axis_index("section") == 0
    kept_rows = jnp.logical_or(keep_mask == 1, jnp.logical_not(is_first))
    inputs = jnp.where(kept_rows[:, None], arriving[0], mask_vector[None, :])
    saved = stashed[0]
    upstream = cotangent[0]
    gain_row = gain[0].astype(jnp.float32)[None, :]
    down_local = down_adapter[0]
    up_local = up_adapter[0]
    width = inputs.shape[1]
    full_width = width * lax.axis_size("mp")
    replicas = lax.axis_size("dp")

    down_mine = lax.dynamic_slice_in_dim(down_local, half * width, width, axis=0)
    down_theirs = lax.dynamic_slice_in_dim(down_local, (1 - half) * width, width, axis=0)
    up_mine = lax.dynamic_slice_in_dim(up_local, half * width, width, axis=1)
    up_theirs = lax.dynamic_slice_in_dim(up_local, (1 - half) * width, width, axis=1)
    down_half = in_unit_order(down_mine, swapped(down_theirs, "mp"), first, 1)
    up_half = in_unit_order(up_mine, swapped(up_theirs, "mp"), first, 0)

    input_values = inputs.astype(jnp.float32)
    saved_values = saved.astype(jnp.float32)
    squares = pair_sum(
        jnp.stack(
            [jnp.sum(input_values * input_values, axis=1), jnp.sum(saved_values * saved_values, axis=1)]
        ),
        "mp",
    )
    scale = lax.rsqrt(squares[0] / full_width + 1e-05)[:, None]
    saved_scale = lax.rsqrt(squares[1] / full_width + 1e-05)[:, None]
    normed = (input_values * scale * gain_row).astype(jnp.bfloat16)
    saved_normed = (saved_values * saved_scale * gain_row).astype(jnp.bfloat16)

    down_partials = pair_sum(
        jnp.stack(
            [
                jnp.dot(normed, down_half, preferred_element_type=jnp.float32),
                jnp.dot(saved_normed, down_half, preferred_element_type=jnp.float32),
            ]
        ),
        "mp",
    )
    hidden_pre, saved_pre = down_partials[0], down_partials[1]
    hidden_grad = pair_sum(contract_cols(upstream, up_half), "mp")
    hidden = jax.nn.silu(hidden_pre).astype(jnp.bfloat16)
    branch = jnp.dot(hidden, up_half, preferred_element_type=jnp.float32)
    output = (input_values + branch).astype(jnp.bfloat16)

    sigmoid_pre = jax.nn.sigmoid(saved_pre)
    saved_hidden = (saved_pre * sigmoid_pre).astype(jnp.bfloat16)
    pre_grad = (hidden_grad * sigmoid_pre * (1.0 + saved_pre * (1.0 - sigmoid_pre))).astype(
        jnp.bfloat16
    )
    scaled_grad = contract_cols(pre_grad, down_half) * gain_row
    row_dot = pair_sum(jnp.sum(saved_values * scaled_grad, axis=1), "mp")
    cubed = saved_scale * saved_scale * saved_scale
    input_grad = (
        upstream.astype(jnp.float32)
        + saved_scale * scaled_grad
        - saved_values * cubed * (row_dot[:, None] / full_width)
    ).astype(jnp.bfloat16)
    next_input = shifted(output, "section", 1)
    prev_grad = shifted(input_grad, "section", -1)

    blocks = replicas // 2
    units = down_local.shape[1]
    block = full_width // replicas
    ny = 4
    nz = replicas // ny
    tokens = saved.shape[0]
    rows = jnp.stack([saved_normed, upstream])
    rows = rows.reshape(2, tokens, nz // 2, ny, block).transpose(3, 2, 0, 1, 4)
    rows = jnp.broadcast_to(rows[:, None], (ny, 2, nz // 2, 2, tokens, block))
    cols = jnp.stack([pre_grad, saved_hidden])
    cols = cols.reshape(2, tokens, 2, units).transpose(2, 0, 1, 3)
    cols = jnp.broadcast_to(cols[None, :, None], (ny, 2, nz // 2, 2, tokens, units))
    slots = lax.dot_general(
        rows, cols, (((4,), (4,)), ((0, 1, 2, 3), (0, 1, 2, 3))), preferred_element_type=jnp.float32
    )
    y_groups = [[z * ny + y for y in range(ny)] for z in range(nz)]
    z_groups = [[z * ny + y for z in range(nz)] for y in range(ny)]
    over_y = lax.all_to_all(
        slots, "dp", 0, 0, tiled=True, axis_index_groups=y_groups
    ).sum(axis=0)
    summed = lax.all_to_all(
        over_y.reshape(nz, 2, block, units), "dp", 0, 0, tiled=True, axis_index_groups=z_groups
    ).sum(axis=0)
    slot = lax.axis_index("dp")
    keeps = (slot // blocks) == half
    pairs = []
    for j in range(replicas):
        for m in range(2):
            if j // blocks != m:
                pairs.append((j * 2 + m, (j ^ blocks) * 2 + (1 - m)))
    moved = lax.ppermute(summed, ("dp", "mp"), pairs)
    mine = jnp.where(keeps, summed, moved) * (1.0 / replicas)
    down_grad = mine[0]
    up_grad = mine[1].T
    return (next_input[None], prev_grad[None], down_grad[None], up_grad[None])


def solution(mesh):
    placed = (
        P("section", "dp", "mp"),
        P("dp"),
        P("mp"),
        P("section", "dp", "mp"),
        P("section", "dp", "mp"),
        P("section", "mp"),
        P("section", None, "mp"),
        P("section", "mp", None),
    )
    return jax.shard_map(
        on_device,
        mesh=mesh,
        in_specs=placed,
        out_specs=(
            P("section", "dp", "mp"),
            P("section", "dp", "mp"),
            P("section", "dp", "mp"),
            P("section", "mp", "dp"),
        ),
        check_vma=False,
    )
```

```python
import jax
import jax.numpy as jnp
from jax import lax
from jax.sharding import PartitionSpec as P


def shifted(shard, axis, by):
    peers = lax.axis_size(axis)
    pairs = [(i, i + by) for i in range(peers) if 0 <= i + by < peers]
    return lax.ppermute(shard, axis, pairs)


def swapped(shard, axis):
    return lax.ppermute(shard, axis, [(0, 1), (1, 0)])


def pair_sum(shard, axis):
    return shard + swapped(shard, axis)


def contract_cols(left, right):
    return lax.dot_general(
        left, right, (((1,), (1,)), ((), ())), preferred_element_type=jnp.float32
    )


def in_unit_order(own, received, first, axis):
    return jnp.where(
        first,
        jnp.concatenate([own, received], axis=axis),
        jnp.concatenate([received, own], axis=axis),
    )


def step(arriving, keep_mask, mask_vector, stashed, cotangent, gain, down_adapter, up_adapter):
    half = lax.axis_index("mp")
    first = half == 0
    is_first = lax.axis_index("section") == 0
    kept_rows = jnp.logical_or(keep_mask == 1, jnp.logical_not(is_first))
    inputs = jnp.where(kept_rows[:, None], arriving[0], mask_vector[None, :])
    saved = stashed[0]
    upstream = cotangent[0]
    gain_row = gain[0].astype(jnp.float32)[None, :]
    down_local = down_adapter[0]
    up_local = up_adapter[0]
    width = inputs.shape[1]
    full_width = width * lax.axis_size("mp")
    replicas = lax.axis_size("dp")

    down_mine = lax.dynamic_slice_in_dim(down_local, half * width, width, axis=0)
    down_theirs = lax.dynamic_slice_in_dim(down_local, (1 - half) * width, width, axis=0)
    up_mine = lax.dynamic_slice_in_dim(up_local, half * width, width, axis=1)
    up_theirs = lax.dynamic_slice_in_dim(up_local, (1 - half) * width, width, axis=1)
    down_received = swapped(down_theirs, "mp")
    up_received = swapped(up_theirs, "mp")
    down_half = in_unit_order(down_mine, down_received, first, 1)
    up_half = in_unit_order(up_mine, up_received, first, 0)

    input_values = inputs.astype(jnp.float32)
    saved_values = saved.astype(jnp.float32)
    squares = jnp.stack(
        [jnp.sum(input_values * input_values, axis=1), jnp.sum(saved_values * saved_values, axis=1)]
    )
    squares = pair_sum(squares, "mp")
    scale = lax.rsqrt(squares[0] / full_width + 1e-05)[:, None]
    saved_scale = lax.rsqrt(squares[1] / full_width + 1e-05)[:, None]
    normed = (input_values * scale * gain_row).astype(jnp.bfloat16)
    saved_normed = (saved_values * saved_scale * gain_row).astype(jnp.bfloat16)

    down_partials = pair_sum(
        jnp.stack(
            [
                jnp.dot(normed, down_half, preferred_element_type=jnp.float32),
                jnp.dot(saved_normed, down_half, preferred_element_type=jnp.float32),
            ]
        ),
        "mp",
    )
    hidden_pre, saved_pre = down_partials[0], down_partials[1]
    hidden_grad = pair_sum(contract_cols(upstream, up_half), "mp")
    hidden = jax.nn.silu(hidden_pre).astype(jnp.bfloat16)
    branch = jnp.dot(hidden, up_half, preferred_element_type=jnp.float32)
    output = (input_values + branch).astype(jnp.bfloat16)

    sigmoid_pre = jax.nn.sigmoid(saved_pre)
    saved_hidden = (saved_pre * sigmoid_pre).astype(jnp.bfloat16)
    pre_grad = (hidden_grad * sigmoid_pre * (1.0 + saved_pre * (1.0 - sigmoid_pre))).astype(
        jnp.bfloat16
    )
    scaled_grad = contract_cols(pre_grad, down_half) * gain_row
    row_dot = pair_sum(jnp.sum(saved_values * scaled_grad, axis=1), "mp")
    cubed = saved_scale * saved_scale * saved_scale
    input_grad = (
        upstream.astype(jnp.float32)
        + saved_scale * scaled_grad
        - saved_values * cubed * (row_dot[:, None] / full_width)
    ).astype(jnp.bfloat16)
    next_input = shifted(output, "section", 1)
    prev_grad = shifted(input_grad, "section", -1)

    blocks = replicas // 2
    units = down_local.shape[1]
    block = full_width // replicas
    ny = 4
    nz = replicas // ny
    tokens = saved.shape[0]
    rows = jnp.stack([saved_normed, upstream])
    rows = rows.reshape(2, tokens, nz // 2, ny, block).transpose(3, 2, 0, 1, 4)
    rows = jnp.broadcast_to(rows[:, None], (ny, 2, nz // 2, 2, tokens, block))
    cols = jnp.stack([pre_grad, saved_hidden])
    cols = cols.reshape(2, tokens, 2, units).transpose(2, 0, 1, 3)
    cols = jnp.broadcast_to(cols[None, :, None], (ny, 2, nz // 2, 2, tokens, units))
    slots = lax.dot_general(
        rows, cols, (((4,), (4,)), ((0, 1, 2, 3), (0, 1, 2, 3))), preferred_element_type=jnp.float32
    )
    y_groups = [[z * ny + y for y in range(ny)] for z in range(nz)]
    z_groups = [[z * ny + y for z in range(nz)] for y in range(ny)]
    over_y = lax.all_to_all(
        slots, "dp", 0, 0, tiled=True, axis_index_groups=y_groups
    ).sum(axis=0)
    summed = lax.all_to_all(
        over_y.reshape(nz, 2, block, units), "dp", 0, 0, tiled=True, axis_index_groups=z_groups
    ).sum(axis=0)
    slot = lax.axis_index("dp")
    keeps = (slot // blocks) == half
    pairs = []
    for j in range(replicas):
        for m in range(2):
            if j // blocks != m:
                pairs.append((j * 2 + m, (j ^ blocks) * 2 + (1 - m)))
    moved = lax.ppermute(summed, ("dp", "mp"), pairs)
    mine = jnp.where(keeps, summed, moved) * (1.0 / replicas)
    down_grad = mine[0]
    up_grad = mine[1].T
    return (next_input[None], prev_grad[None], down_grad[None], up_grad[None])


def solution(mesh):
    placed = (
        P("section", "dp", "mp"),
        P("dp"),
        P("mp"),
        P("section", "dp", "mp"),
        P("section", "dp", "mp"),
        P("section", "mp"),
        P("section", None, "mp"),
        P("section", "mp", None),
    )
    return jax.shard_map(
        step,
        mesh=mesh,
        in_specs=placed,
        out_specs=(
            P("section", "dp", "mp"),
            P("section", "dp", "mp"),
            P("section", "dp", "mp"),
            P("section", "mp", "dp"),
        ),
        check_vma=False,
    )
```

```python
import jax
import jax.numpy as jnp
from jax import lax
from jax.sharding import PartitionSpec as P


def shifted(shard, axis, by):
    peers = lax.axis_size(axis)
    pairs = [(i, i + by) for i in range(peers) if 0 <= i + by < peers]
    return lax.ppermute(shard, axis, pairs)


def swapped(shard, axis):
    return lax.ppermute(shard, axis, [(0, 1), (1, 0)])


def pair_sum(shard, axis):
    return shard + swapped(shard, axis)


def contract_cols(left, right):
    return lax.dot_general(
        left, right, (((1,), (1,)), ((), ())), preferred_element_type=jnp.float32
    )


def in_unit_order(own, received, first, axis):
    return jnp.where(
        first,
        jnp.concatenate([own, received], axis=axis),
        jnp.concatenate([received, own], axis=axis),
    )


def step(arriving, keep_mask, mask_vector, stashed, cotangent, gain, down_adapter, up_adapter):
    half = lax.axis_index("mp")
    first = half == 0
    is_first = lax.axis_index("section") == 0
    kept_rows = jnp.logical_or(keep_mask == 1, jnp.logical_not(is_first))
    inputs = jnp.where(kept_rows[:, None], arriving[0], mask_vector[None, :])
    saved = stashed[0]
    upstream = cotangent[0]
    gain_row = gain[0].astype(jnp.float32)[None, :]
    down_local = down_adapter[0]
    up_local = up_adapter[0]
    width = inputs.shape[1]
    full_width = width * lax.axis_size("mp")
    replicas = lax.axis_size("dp")

    down_mine = lax.dynamic_slice_in_dim(down_local, half * width, width, axis=0)
    down_theirs = lax.dynamic_slice_in_dim(down_local, (1 - half) * width, width, axis=0)
    up_mine = lax.dynamic_slice_in_dim(up_local, half * width, width, axis=1)
    up_theirs = lax.dynamic_slice_in_dim(up_local, (1 - half) * width, width, axis=1)
    down_half = in_unit_order(down_mine, swapped(down_theirs, "mp"), first, 1)
    up_received = swapped(up_theirs, "mp")
    up_half = in_unit_order(up_mine, up_received, first, 0)

    input_values = inputs.astype(jnp.float32)
    saved_values = saved.astype(jnp.float32)
    squares = pair_sum(
        jnp.stack(
            [jnp.sum(input_values * input_values, axis=1), jnp.sum(saved_values * saved_values, axis=1)]
        ),
        "mp",
    )
    scale = lax.rsqrt(squares[0] / full_width + 1e-05)[:, None]
    saved_scale = lax.rsqrt(squares[1] / full_width + 1e-05)[:, None]
    normed = (input_values * scale * gain_row).astype(jnp.bfloat16)
    saved_normed = (saved_values * saved_scale * gain_row).astype(jnp.bfloat16)

    down_partials = pair_sum(
        jnp.stack(
            [
                jnp.dot(normed, down_half, preferred_element_type=jnp.float32),
                jnp.dot(saved_normed, down_half, preferred_element_type=jnp.float32),
            ]
        ),
        "mp",
    )
    hidden_pre, saved_pre = down_partials[0], down_partials[1]
    hidden_grad = pair_sum(contract_cols(upstream, up_half), "mp")
    hidden = jax.nn.silu(hidden_pre).astype(jnp.bfloat16)
    branch = jnp.dot(hidden, up_half, preferred_element_type=jnp.float32)
    output = (input_values + branch).astype(jnp.bfloat16)

    sigmoid_pre = jax.nn.sigmoid(saved_pre)
    saved_hidden = (saved_pre * sigmoid_pre).astype(jnp.bfloat16)
    pre_grad = (hidden_grad * sigmoid_pre * (1.0 + saved_pre * (1.0 - sigmoid_pre))).astype(
        jnp.bfloat16
    )
    scaled_grad = contract_cols(pre_grad, down_half) * gain_row
    row_dot = pair_sum(jnp.sum(saved_values * scaled_grad, axis=1), "mp")
    cubed = saved_scale * saved_scale * saved_scale
    input_grad = (
        upstream.astype(jnp.float32)
        + saved_scale * scaled_grad
        - saved_values * cubed * (row_dot[:, None] / full_width)
    ).astype(jnp.bfloat16)
    next_input = shifted(output, "section", 1)
    prev_grad = shifted(input_grad, "section", -1)

    blocks = replicas // 2
    units = down_local.shape[1]
    block = full_width // replicas
    ny = 4
    nz = replicas // ny
    tokens = saved.shape[0]
    y_groups = [[z * ny + y for y in range(ny)] for z in range(nz)]
    z_groups = [[z * ny + y for z in range(nz)] for y in range(ny)]

    def summed_over_y(rows, cols):
        rows = rows.reshape(tokens, nz // 2, ny, block).transpose(2, 1, 0, 3)
        rows = jnp.broadcast_to(rows[:, None], (ny, 2, nz // 2, tokens, block))
        cols = cols.reshape(tokens, 2, units).transpose(1, 0, 2)
        cols = jnp.broadcast_to(cols[None, :, None], (ny, 2, nz // 2, tokens, units))
        slots = lax.dot_general(
            rows, cols, (((3,), (3,)), ((0, 1, 2), (0, 1, 2))), preferred_element_type=jnp.float32
        )
        return lax.all_to_all(slots, "dp", 0, 0, tiled=True, axis_index_groups=y_groups).sum(axis=0)

    up_over_y = summed_over_y(upstream, saved_hidden)
    down_over_y = summed_over_y(saved_normed, pre_grad)
    over_y = jnp.stack([down_over_y, up_over_y], axis=2)
    summed = lax.all_to_all(
        over_y.reshape(nz, 2, block, units), "dp", 0, 0, tiled=True, axis_index_groups=z_groups
    ).sum(axis=0)
    slot = lax.axis_index("dp")
    keeps = (slot // blocks) == half
    pairs = []
    for j in range(replicas):
        for m in range(2):
            if j // blocks != m:
                pairs.append((j * 2 + m, (j ^ blocks) * 2 + (1 - m)))
    moved = lax.ppermute(summed, ("dp", "mp"), pairs)
    mine = jnp.where(keeps, summed, moved) * (1.0 / replicas)
    down_grad = mine[0]
    up_grad = mine[1].T
    return (next_input[None], prev_grad[None], down_grad[None], up_grad[None])


def solution(mesh):
    placed = (
        P("section", "dp", "mp"),
        P("dp"),
        P("mp"),
        P("section", "dp", "mp"),
        P("section", "dp", "mp"),
        P("section", "mp"),
        P("section", None, "mp"),
        P("section", "mp", None),
    )
    return jax.shard_map(
        step,
        mesh=mesh,
        in_specs=placed,
        out_specs=(
            P("section", "dp", "mp"),
            P("section", "dp", "mp"),
            P("section", "dp", "mp"),
            P("section", "mp", "dp"),
        ),
        check_vma=False,
    )
```
